256 devices in a mesh: row: 8 (over y, core), col: 32 (over z, x).
Axes of the slice: x: 4, y: 4, z: 8, core: 2. Of those that a mesh axis runs over, the one named last changes fastest.
Arguments:
- prior_solved: bfloat16 [92160, 768], P('col'), may hold values from -6 to 6
- lower_prior: bfloat16 [92160, 2, 3072], P('col', None, 'row'), may hold values from -0.01953125 to 0.01953125
- rhs: bfloat16 [2, 3072, 768], P(None, 'row'), may hold values from -6 to 6
- coupling: bfloat16 [3072, 3072], P('col', 'row'), may hold values from -0.109375 to 0.109375
- inverse_diag: bfloat16 [2, 3072, 3072], P(None, 'col', 'row'), may hold values from -1 to 1, as said below
Outputs:
- solved: bfloat16 [2, 3072, 768], P(None, 'row')
The draws below stay inside these ranges and needn't reach their ends.
Inputs may be any that keep to these rules, and one draw needn't show every extreme that they name: Each block inverse_diag[b] is the inverse of a unit lower triangular block: entry [b, j, i] is zero for j > i and exactly one for j == i.
All inputs are finite; a program needn't handle non-finite values.
Results may differ from the reference program's by a relative error of at most 0.0056.
Values may be sent and summed in bfloat16 or wider, within the bound.
No kernel may reach another device: no remote copies, remote signals or barrier semaphores. Data moves between devices by JAX's collectives and lax.ppermute only.
A program may use at most 64 MiB of HBM per device.

```python
import math
import jax
import jax.numpy as jnp
from jax import lax

NB = 3072
RHS = 768
PRIOR = 92160


def draw_inverse_diag(key, part):
    noise_field = jax.random.normal(key, (2, NB, NB), jnp.float32)
    row_ids = lax.broadcasted_iota(jnp.int32, (NB, NB), 0)
    col_ids = lax.broadcasted_iota(jnp.int32, (NB, NB), 1)
    lower_mask = (row_ids < col_ids).astype(jnp.float32)
    unit_diag = (row_ids == col_ids).astype(jnp.float32)
    values = noise_field * lower_mask * (0.6 / math.sqrt(NB)) + unit_diag
    return values.astype(jnp.bfloat16)


def block_scale(rng, extent, split, least, high):
    def one(position, parts):
        draws = jax.random.uniform(jax.random.fold_in(jax.random.fold_in(rng, 6), position), (parts,), jnp.float32, least / len(split), high / len(split))
        return jnp.repeat(jnp.exp(draws), extent[position] // parts).reshape((-1,) + (1,) * (len(extent) - position - 1))

    loudness = one(*split[0])
    for cut in split[1:]:
        loudness = loudness * one(*cut)
    return loudness


def gaussian(key, shape, scale, reach, pieces=(), held_as=jnp.bfloat16):
    result = scale * jax.random.normal(key, shape, jnp.float32)
    if pieces:
        result = result * block_scale(key, shape, pieces, -0.22, 0.18)
    return jnp.clip(result, -reach, reach).astype(held_as)


def setup_inputs(seed: int = 0) -> dict:
    key_of = jax.random.split(jax.random.key(seed), 6)
    return {
        "prior_solved": gaussian(key_of[0], (PRIOR, RHS), 1.0, 6.0, ((0, 32),)),
        "lower_prior": gaussian(key_of[1], (PRIOR, 2, NB), PRIOR ** -0.5, 0.01953125, ((0, 32), (2, 8))),
        "rhs": gaussian(key_of[2], (2, NB, RHS), 1.0, 6.0, ((1, 8),)),
        "coupling": gaussian(key_of[3], (NB, NB), NB ** -0.5, 0.109375, ((0, 32), (1, 8))),
        "inverse_diag": draw_inverse_diag(jax.random.fold_in(key_of[5], 71), 0),
    }


def block_sum(lower_prior, prior_solved, block_id):
    return jnp.dot(lower_prior[:, block_id, :].T, prior_solved, preferred_element_type=jnp.float32)


def reference(prior_solved, lower_prior, rhs, coupling, inverse_diag):
    first_sum = block_sum(lower_prior, prior_solved, 0)
    second_sum = block_sum(lower_prior, prior_solved, 1)
    first_reduced = (rhs[0].astype(jnp.float32) - first_sum).astype(jnp.bfloat16)
    first_solved = jnp.dot(inverse_diag[0].T, first_reduced, preferred_element_type=jnp.float32).astype(jnp.bfloat16)
    cross_term = jnp.dot(coupling.T, first_solved, preferred_element_type=jnp.float32)
    second_reduced = (rhs[1].astype(jnp.float32) - second_sum - cross_term).astype(jnp.bfloat16)
    second_solved = jnp.dot(inverse_diag[1].T, second_reduced, preferred_element_type=jnp.float32).astype(jnp.bfloat16)
    return jnp.stack([first_solved, second_solved])
```

```python
import jax
import jax.numpy as jnp
from jax import lax
from jax.sharding import PartitionSpec as P


def in_blocks(array, dim, length):
    dims = array.shape
    blocks = array.reshape(*dims[:dim], length, dims[dim] // length, *dims[dim + 1 :])
    return jnp.moveaxis(blocks, dim, 0)


def sum_at_owner(array, axis, dim):
    length = lax.axis_size(axis)
    blocks = lax.all_to_all(in_blocks(array, dim, length), axis, 0, 0, tiled=True)
    return jnp.sum(blocks, axis=0)


def in_order(blocks, dim):
    blocks = jnp.moveaxis(blocks, 0, dim)
    dims = blocks.shape
    return blocks.reshape(*dims[:dim], dims[dim] * dims[dim + 1], *dims[dim + 2 :])


def sent_to_all(array, axis):
    copies = jnp.broadcast_to(array, (lax.axis_size(axis), *array.shape))
    return lax.all_to_all(copies, axis, split_axis=0, concat_axis=0, tiled=True)


def collect(array, axis, dim):
    return in_order(sent_to_all(array, axis), dim)


def local_product(left_block, right_rows):
    return lax.dot_general(
        left_block, right_rows, (((0,), (0,)), ((), ())), preferred_element_type=jnp.float32
    )


def on_device(prior_solved, lower_prior, rhs, coupling, inverse_diag):
    share_width = rhs.shape[2] // lax.axis_size("col")
    share_start = lax.axis_index("col") * share_width
    depth, blocks, rows = lower_prior.shape
    both_terms = local_product(lower_prior.reshape(depth, blocks * rows), prior_solved)
    both_terms = both_terms.reshape(blocks, rows, rhs.shape[2])
    first_share = sum_at_owner(both_terms[0], "col", 1)
    second_share = sum_at_owner(both_terms[1], "col", 1)
    first_block = lax.all_gather(inverse_diag[0], "col", axis=0, tiled=True)
    cross_block = lax.all_gather(coupling, "col", axis=0, tiled=True)
    second_block = lax.all_gather(inverse_diag[1], "col", axis=0, tiled=True)
    rhs_share = lax.dynamic_slice_in_dim(rhs, share_start, share_width, 2).astype(jnp.float32)

    def apply_share(left_block, vector_rows):
        full_vector = collect(vector_rows, "row", 0)
        return local_product(left_block, full_vector)

    first_reduced = (rhs_share[0] - first_share).astype(jnp.bfloat16)
    first_solved = apply_share(first_block, first_reduced).astype(jnp.bfloat16)
    first_out = collect(first_solved, "col", 1)
    cross_term = apply_share(cross_block, first_solved)
    second_reduced = (rhs_share[1] - second_share - cross_term).astype(jnp.bfloat16)
    second_solved = apply_share(second_block, second_reduced).astype(jnp.bfloat16)
    second_out = collect(second_solved, "col", 1)
    return jnp.stack([first_out, second_out])


def solution(mesh):
    return jax.shard_map(
        on_device,
        mesh=mesh,
        in_specs=(
            P("col", None),
            P("col", None, "row"),
            P(None, "row", None),
            P("col", "row"),
            P(None, "col", "row"),
        ),
        out_specs=P(None, "row", None),
        check_vma=False,
    )
```

```python
import jax
import jax.numpy as jnp
from jax import lax
from jax.sharding import Mesh, PartitionSpec as P

COL = ("z", "x")


def sent_to_all(array, axis, length):
    copies = jnp.broadcast_to(array, (length, *array.shape))
    return lax.all_to_all(copies, axis, split_axis=0, concat_axis=0, tiled=True)


def left_product(left_block, right_rows):
    return lax.dot_general(
        left_block, right_rows, (((0,), (0,)), ((), ())), preferred_element_type=jnp.float32
    )


def on_device(prior_solved, lower_prior, rhs, coupling, inverse_diag):
    nrow = lax.axis_size("row")
    nz = lax.axis_size("z")
    nx = lax.axis_size("x")
    depth, blocks, rows = lower_prior.shape
    width = rhs.shape[2]
    piece = rows // nz
    quarter = width // nx
    zi = lax.axis_index("z")
    xi = lax.axis_index("x")

    stacked = jnp.stack([inverse_diag[0], coupling, inverse_diag[1]])
    tiles = lax.all_gather(stacked, "x", axis=1, tiled=True)

    both_terms = left_product(lower_prior.reshape(depth, blocks * rows), prior_solved)
    both_terms = both_terms.reshape(blocks, nz, piece, nx, quarter)

    def prior_share(b):
        chunks = jnp.swapaxes(both_terms[b], 1, 2).reshape(nz * nx, piece, quarter)
        return jnp.sum(lax.all_to_all(chunks, COL, 0, 0, tiled=True), axis=0)

    def sum_over_z(partial):
        chunks = partial.reshape(nz, piece, quarter)
        return jnp.sum(lax.all_to_all(chunks, "z", 0, 0, tiled=True), axis=0)

    transpose = [(r * nz + z, z * nz + r) for r in range(nrow) for z in range(nz)]

    def as_input(piece_rows):
        moved = lax.ppermute(piece_rows, ("row", "z"), transpose)
        return sent_to_all(moved, "row", nrow).reshape(rows, quarter)

    rhs_share = lax.dynamic_slice(rhs, (0, zi * piece, xi * quarter), (blocks, piece, quarter))
    rhs_share = rhs_share.astype(jnp.float32)

    first_share = prior_share(0)
    second_share = prior_share(1)
    first_reduced = (rhs_share[0] - first_share).astype(jnp.bfloat16)
    first_solved = sum_over_z(left_product(tiles[0], as_input(first_reduced))).astype(jnp.bfloat16)
    first_out = sent_to_all(first_solved, COL, nz * nx)
    cross_term = sum_over_z(left_product(tiles[1], as_input(first_solved)))
    second_reduced = (rhs_share[1] - second_share - cross_term).astype(jnp.bfloat16)
    second_solved = sum_over_z(left_product(tiles[2], as_input(second_reduced))).astype(jnp.bfloat16)
    second_out = sent_to_all(second_solved, COL, nz * nx)
    out = jnp.stack([first_out, second_out], axis=1)
    out = out.reshape(nz, nx, blocks, piece, quarter)
    return jnp.transpose(out, (2, 0, 3, 1, 4)).reshape(blocks, rows, width)


def solution(mesh):
    nrow, ncol = mesh.devices.shape
    nz = nrow
    fine = Mesh(mesh.devices.reshape(nrow, nz, ncol // nz), ("row", "z", "x"))
    return jax.shard_map(
        on_device,
        mesh=fine,
        in_specs=(
            P(COL, None),
            P(COL, None, "row"),
            P(None, "row", None),
            P(COL, "row"),
            P(None, COL, "row"),
        ),
        out_specs=P(None, "row", None),
        check_vma=False,
    )
```

```python
import jax
import jax.numpy as jnp
from jax import lax
from jax.sharding import Mesh, PartitionSpec as P

COL = ("z", "x")


def sent_to_all(array, axis, length):
    copies = jnp.broadcast_to(array, (length, *array.shape))
    return lax.all_to_all(copies, axis, split_axis=0, concat_axis=0, tiled=True)


def left_product(left_block, right_rows):
    return lax.dot_general(
        left_block, right_rows, (((0,), (0,)), ((), ())), preferred_element_type=jnp.float32
    )


def on_device(prior_solved, lower_prior, rhs, coupling, inverse_diag):
    nrow = lax.axis_size("row")
    nz = lax.axis_size("z")
    nx = lax.axis_size("x")
    ncol = nz * nx
    depth, blocks, rows = lower_prior.shape
    width = rhs.shape[2]
    piece = rows // nz
    quarter = width // nx
    share = quarter // nz
    zi = lax.axis_index("z")
    xi = lax.axis_index("x")

    later_blocks = lax.all_gather(jnp.stack([coupling, inverse_diag[1]]), COL, axis=1, tiled=True)
    first_tile = lax.all_gather(inverse_diag[0], "x", axis=0, tiled=True)

    both_terms = left_product(lower_prior.reshape(depth, blocks * rows), prior_solved)
    both_terms = both_terms.reshape(blocks, rows, width).astype(jnp.bfloat16)
    first_chunks = both_terms[0].reshape(nz, piece, nx, quarter).transpose(0, 2, 1, 3)
    second_chunks = both_terms[1].reshape(rows, nx, nz, share).transpose(2, 1, 0, 3)
    chunks = jnp.concatenate(
        [first_chunks.reshape(ncol, piece * quarter), second_chunks.reshape(ncol, rows * share)], axis=1
    )
    sums = jnp.sum(lax.all_to_all(chunks, COL, 0, 0, tiled=True).astype(jnp.float32), axis=0)
    first_share = sums[: piece * quarter].reshape(piece, quarter)
    second_share = sums[piece * quarter :].reshape(rows, share)

    rhs_first = lax.dynamic_slice(rhs[0], (zi * piece, xi * quarter), (piece, quarter))
    rhs_second = lax.dynamic_slice(rhs[1], (0, xi * quarter + zi * share), (rows, share))

    transpose = [(r * nz + z, z * nz + r) for r in range(nrow) for z in range(nz)]

    def as_tile_input(piece_rows):
        moved = lax.ppermute(piece_rows, ("row", "z"), transpose)
        return sent_to_all(moved, "row", nrow).reshape(rows, quarter)

    def as_full_input(share_rows):
        return sent_to_all(share_rows, "row", nrow).reshape(nrow * rows, share)

    def output_rows(share_rows):
        got = sent_to_all(share_rows, COL, ncol).reshape(nz, nx, rows, share)
        return got.transpose(2, 1, 0, 3).reshape(rows, width)

    first_reduced = (rhs_first.astype(jnp.float32) - first_share).astype(jnp.bfloat16)
    partial = left_product(first_tile, as_tile_input(first_reduced)).reshape(nz, piece, quarter)
    first_piece = jnp.sum(lax.all_to_all(partial, "z", 0, 0, tiled=True), axis=0).astype(jnp.bfloat16)
    split = first_piece.reshape(piece, nz, share).transpose(1, 0, 2)
    first_solved = lax.all_to_all(split, "z", 0, 0, tiled=True).reshape(rows, share)
    first_out = output_rows(first_solved)

    cross_term = left_product(later_blocks[0], as_full_input(first_solved))
    second_reduced = (rhs_second.astype(jnp.float32) - second_share - cross_term).astype(jnp.bfloat16)
    second_solved = left_product(later_blocks[1], as_full_input(second_reduced)).astype(jnp.bfloat16)
    second_out = output_rows(second_solved)
    return jnp.stack([first_out, second_out])


def solution(mesh):
    nrow, ncol = mesh.devices.shape
    nz = nrow
    fine = Mesh(mesh.devices.reshape(nrow, nz, ncol // nz), ("row", "z", "x"))
    return jax.shard_map(
        on_device,
        mesh=fine,
        in_specs=(
            P(COL, None),
            P(COL, None, "row"),
            P(None, "row", None),
            P(COL, "row"),
            P(None, COL, "row"),
        ),
        out_specs=P(None, "row", None),
        check_vma=False,
    )
```

```python
import jax
import jax.numpy as jnp
from jax import lax
from jax.sharding import PartitionSpec as P


def in_blocks(array, dim, length):
    dims = array.shape
    blocks = array.reshape(*dims[:dim], length, dims[dim] // length, *dims[dim + 1 :])
    return jnp.moveaxis(blocks, dim, 0)


def sum_at_owner(array, axis, dim):
    length = lax.axis_size(axis)
    blocks = lax.all_to_all(in_blocks(array, dim, length), axis, 0, 0, tiled=True)
    return jnp.sum(blocks, axis=0)


def in_order(blocks, dim):
    blocks = jnp.moveaxis(blocks, 0, dim)
    dims = blocks.shape
    return blocks.reshape(*dims[:dim], dims[dim] * dims[dim + 1], *dims[dim + 2 :])


def sent_to_all(array, axis):
    copies = jnp.broadcast_to(array, (lax.axis_size(axis), *array.shape))
    return lax.all_to_all(copies, axis, split_axis=0, concat_axis=0, tiled=True)


def collect(array, axis, dim):
    return in_order(sent_to_all(array, axis), dim)


def local_product(left_block, right_rows):
    return lax.dot_general(
        left_block, right_rows, (((0,), (0,)), ((), ())), preferred_element_type=jnp.float32
    )


def on_device(prior_solved, lower_prior, rhs, coupling, inverse_diag):
    share_width = rhs.shape[2] // lax.axis_size("col")
    share_start = lax.axis_index("col") * share_width
    stacked = jnp.concatenate([inverse_diag, coupling[None]], axis=0)
    whole_blocks = lax.all_gather(stacked, "col", axis=1, tiled=True)
    depth, blocks, rows = lower_prior.shape
    both_terms = local_product(lower_prior.reshape(depth, blocks * rows), prior_solved)
    both_terms = both_terms.reshape(blocks, rows, rhs.shape[2])
    shares = sum_at_owner(both_terms, "col", 2)
    rhs_share = lax.dynamic_slice_in_dim(rhs, share_start, share_width, 2).astype(jnp.float32)

    def apply_share(left_block, vector_rows):
        full_vector = collect(vector_rows, "row", 0)
        return local_product(left_block, full_vector)

    first_reduced = (rhs_share[0] - shares[0]).astype(jnp.bfloat16)
    first_solved = apply_share(whole_blocks[0], first_reduced).astype(jnp.bfloat16)
    first_out = collect(first_solved, "col", 1)
    cross_term = apply_share(whole_blocks[2], first_solved)
    second_reduced = (rhs_share[1] - shares[1] - cross_term).astype(jnp.bfloat16)
    second_solved = apply_share(whole_blocks[1], second_reduced).astype(jnp.bfloat16)
    second_out = collect(second_solved, "col", 1)
    return jnp.stack([first_out, second_out])


def solution(mesh):
    return jax.shard_map(
        on_device,
        mesh=mesh,
        in_specs=(
            P("col", None),
            P("col", None, "row"),
            P(None, "row", None),
            P("col", "row"),
            P(None, "col", "row"),
        ),
        out_specs=P(None, "row", None),
        check_vma=False,
    )
```

```python
import jax
import jax.numpy as jnp
from jax import lax
from jax.sharding import PartitionSpec as P


def in_blocks(array, dim, length):
    dims = array.shape
    blocks = array.reshape(*dims[:dim], length, dims[dim] // length, *dims[dim + 1 :])
    return jnp.moveaxis(blocks, dim, 0)


def sum_at_owner(array, axis, dim):
    length = lax.axis_size(axis)
    blocks = lax.all_to_all(in_blocks(array, dim, length), axis, 0, 0, tiled=True)
    return jnp.sum(blocks, axis=0)


def in_order(blocks, dim):
    blocks = jnp.moveaxis(blocks, 0, dim)
    dims = blocks.shape
    return blocks.reshape(*dims[:dim], dims[dim] * dims[dim + 1], *dims[dim + 2 :])


def sent_to_all(array, axis):
    copies = jnp.broadcast_to(array, (lax.axis_size(axis), *array.shape))
    return lax.all_to_all(copies, axis, split_axis=0, concat_axis=0, tiled=True)


def collect(array, axis, dim):
    return in_order(sent_to_all(array, axis), dim)


def local_product(left_block, right_rows):
    return lax.dot_general(
        left_block, right_rows, (((0,), (0,)), ((), ())), preferred_element_type=jnp.float32
    )


def on_device(prior_solved, lower_prior, rhs, coupling, inverse_diag):
    share_width = rhs.shape[2] // lax.axis_size("col")
    share_start = lax.axis_index("col") * share_width
    stacked = jnp.concatenate([inverse_diag, coupling[None]], axis=0)
    whole_blocks = lax.all_gather(stacked, "col", axis=1, tiled=True)
    depth, blocks, rows = lower_prior.shape
    both_terms = local_product(lower_prior.reshape(depth, blocks * rows), prior_solved)
    both_terms = both_terms.reshape(blocks, rows, rhs.shape[2])
    shares = sum_at_owner(both_terms, "col", 2)
    rhs_share = lax.dynamic_slice_in_dim(rhs, share_start, share_width, 2).astype(jnp.float32)

    def apply_share(left_block, vector_rows):
        full_vector = collect(vector_rows, "row", 0)
        return local_product(left_block, full_vector)

    first_reduced = (rhs_share[0] - shares[0]).astype(jnp.bfloat16)
    first_solved = apply_share(whole_blocks[0], first_reduced).astype(jnp.bfloat16)
    cross_term = apply_share(whole_blocks[2], first_solved)
    second_reduced = (rhs_share[1] - shares[1] - cross_term).astype(jnp.bfloat16)
    second_solved = apply_share(whole_blocks[1], second_reduced).astype(jnp.bfloat16)
    solved_share = jnp.stack([first_solved, second_solved])
    return collect(solved_share, "col", 2)


def solution(mesh):
    return jax.shard_map(
        on_device,
        mesh=mesh,
        in_specs=(
            P("col", None),
            P("col", None, "row"),
            P(None, "row", None),
            P("col", "row"),
            P(None, "col", "row"),
        ),
        out_specs=P(None, "row", None),
        check_vma=False,
    )
```

```python
import jax
import jax.numpy as jnp
from jax import lax
from jax.sharding import PartitionSpec as P


def in_blocks(array, dim, length):
    dims = array.shape
    blocks = array.reshape(*dims[:dim], length, dims[dim] // length, *dims[dim + 1 :])
    return jnp.moveaxis(blocks, dim, 0)


def sum_at_owner(array, axis, dim):
    length = lax.axis_size(axis)
    blocks = lax.all_to_all(in_blocks(array, dim, length), axis, 0, 0, tiled=True)
    return jnp.sum(blocks, axis=0)


def in_order(blocks, dim):
    blocks = jnp.moveaxis(blocks, 0, dim)
    dims = blocks.shape
    return blocks.reshape(*dims[:dim], dims[dim] * dims[dim + 1], *dims[dim + 2 :])


def sent_to_all(array, axis):
    copies = jnp.broadcast_to(array, (lax.axis_size(axis), *array.shape))
    return lax.all_to_all(copies, axis, split_axis=0, concat_axis=0, tiled=True)


def collect(array, axis, dim):
    flat = array.reshape(array.size // 128, 128)
    got = sent_to_all(flat, axis).reshape(lax.axis_size(axis), *array.shape)
    return in_order(got, dim)


def local_product(left_block, right_rows):
    return lax.dot_general(
        left_block, right_rows, (((0,), (0,)), ((), ())), preferred_element_type=jnp.float32
    )


def on_device(prior_solved, lower_prior, rhs, coupling, inverse_diag):
    share_width = rhs.shape[2] // lax.axis_size("col")
    share_start = lax.axis_index("col") * share_width
    stacked = jnp.concatenate([inverse_diag, coupling[None]], axis=0)
    whole_blocks = lax.all_gather(stacked, "col", axis=1, tiled=True)
    depth, blocks, rows = lower_prior.shape
    both_terms = local_product(lower_prior.reshape(depth, blocks * rows), prior_solved)
    both_terms = both_terms.reshape(blocks, rows, rhs.shape[2])
    shares = sum_at_owner(both_terms, "col", 2)
    rhs_share = lax.dynamic_slice_in_dim(rhs, share_start, share_width, 2).astype(jnp.float32)

    def apply_share(left_block, vector_rows):
        full_vector = collect(vector_rows, "row", 0)
        return local_product(left_block, full_vector)

    first_reduced = (rhs_share[0] - shares[0]).astype(jnp.bfloat16)
    first_solved = apply_share(whole_blocks[0], first_reduced).astype(jnp.bfloat16)
    cross_term = apply_share(whole_blocks[2], first_solved)
    second_reduced = (rhs_share[1] - shares[1] - cross_term).astype(jnp.bfloat16)
    second_solved = apply_share(whole_blocks[1], second_reduced).astype(jnp.bfloat16)
    solved_share = jnp.stack([first_solved, second_solved])
    return collect(solved_share, "col", 2)


def solution(mesh):
    return jax.shard_map(
        on_device,
        mesh=mesh,
        in_specs=(
            P("col", None),
            P("col", None, "row"),
            P(None, "row", None),
            P("col", "row"),
            P(None, "col", "row"),
        ),
        out_specs=P(None, "row", None),
        check_vma=False,
    )
```

```python
import jax
import jax.numpy as jnp
from jax import lax
from jax.sharding import Mesh, PartitionSpec as P

COL = ("z", "x")


def in_blocks(array, dim, length):
    dims = array.shape
    blocks = array.reshape(*dims[:dim], length, dims[dim] // length, *dims[dim + 1 :])
    return jnp.moveaxis(blocks, dim, 0)


def sum_at_owner(array, axis, dim):
    length = lax.axis_size(axis)
    blocks = lax.all_to_all(in_blocks(array, dim, length), axis, 0, 0, tiled=True)
    return jnp.sum(blocks, axis=0)


def in_order(blocks, dim):
    blocks = jnp.moveaxis(blocks, 0, dim)
    dims = blocks.shape
    return blocks.reshape(*dims[:dim], dims[dim] * dims[dim + 1], *dims[dim + 2 :])


def sent_to_all(array, axis):
    copies = jnp.broadcast_to(array, (lax.axis_size(axis), *array.shape))
    return lax.all_to_all(copies, axis, split_axis=0, concat_axis=0, tiled=True)


def collect(array, axis, dim):
    return in_order(sent_to_all(array, axis), dim)


def local_product(left_block, right_rows):
    return lax.dot_general(
        left_block, right_rows, (((0,), (0,)), ((), ())), preferred_element_type=jnp.float32
    )


def on_device(prior_solved, lower_prior, rhs, coupling, inverse_diag):
    share_width = rhs.shape[2] // lax.axis_size(COL)
    share_start = lax.axis_index(COL) * share_width
    stacked = jnp.concatenate([inverse_diag, coupling[None]], axis=0)
    whole_blocks = lax.all_gather(stacked, COL, axis=1, tiled=True)
    depth, blocks, rows = lower_prior.shape
    both_terms = local_product(lower_prior.reshape(depth, blocks * rows), prior_solved)
    both_terms = both_terms.reshape(blocks, rows, rhs.shape[2])
    shares = sum_at_owner(both_terms, COL, 2)
    rhs_share = lax.dynamic_slice_in_dim(rhs, share_start, share_width, 2).astype(jnp.float32)

    def apply_share(left_block, vector_rows):
        full_vector = collect(vector_rows, "row", 0)
        return local_product(left_block, full_vector)

    first_reduced = (rhs_share[0] - shares[0]).astype(jnp.bfloat16)
    first_solved = apply_share(whole_blocks[0], first_reduced).astype(jnp.bfloat16)
    cross_term = apply_share(whole_blocks[2], first_solved)
    second_reduced = (rhs_share[1] - shares[1] - cross_term).astype(jnp.bfloat16)
    second_solved = apply_share(whole_blocks[1], second_reduced).astype(jnp.bfloat16)
    solved_share = jnp.stack([first_solved, second_solved])
    across_x = lax.all_gather(solved_share, "x", axis=2, tiled=True)
    return collect(across_x, "z", 2)


def solution(mesh):
    nrow, ncol = mesh.devices.shape
    fine = Mesh(mesh.devices.reshape(nrow, nrow, ncol // nrow), ("row", "z", "x"))
    return jax.shard_map(
        on_device,
        mesh=fine,
        in_specs=(
            P(COL, None),
            P(COL, None, "row"),
            P(None, "row", None),
            P(COL, "row"),
            P(None, COL, "row"),
        ),
        out_specs=P(None, "row", None),
        check_vma=False,
    )
```

```python
import jax
import jax.numpy as jnp
from jax import lax
from jax.sharding import Mesh, PartitionSpec as P

ROW = ("y", "core")


def in_blocks(array, dim, length):
    dims = array.shape
    blocks = array.reshape(*dims[:dim], length, dims[dim] // length, *dims[dim + 1 :])
    return jnp.moveaxis(blocks, dim, 0)


def sum_at_owner(array, axis, dim):
    length = lax.axis_size(axis)
    blocks = lax.all_to_all(in_blocks(array, dim, length), axis, 0, 0, tiled=True)
    return jnp.sum(blocks, axis=0)


def in_order(blocks, dim):
    blocks = jnp.moveaxis(blocks, 0, dim)
    dims = blocks.shape
    return blocks.reshape(*dims[:dim], dims[dim] * dims[dim + 1], *dims[dim + 2 :])


def sent_to_all(array, axis):
    copies = jnp.broadcast_to(array, (lax.axis_size(axis), *array.shape))
    return lax.all_to_all(copies, axis, split_axis=0, concat_axis=0, tiled=True)


def collect(array, axis, dim):
    return in_order(sent_to_all(array, axis), dim)


def local_product(left_block, right_rows):
    return lax.dot_general(
        left_block, right_rows, (((0,), (0,)), ((), ())), preferred_element_type=jnp.float32
    )


def on_device(prior_solved, lower_prior, rhs, coupling, inverse_diag):
    share_width = rhs.shape[2] // lax.axis_size("col")
    share_start = lax.axis_index("col") * share_width
    stacked = jnp.concatenate([inverse_diag, coupling[None]], axis=0)
    whole_blocks = lax.all_gather(stacked, "col", axis=1, tiled=True)
    depth, blocks, rows = lower_prior.shape
    both_terms = local_product(lower_prior.reshape(depth, blocks * rows), prior_solved)
    both_terms = both_terms.reshape(blocks, rows, rhs.shape[2])
    shares = sum_at_owner(both_terms, "col", 2)
    rhs_share = lax.dynamic_slice_in_dim(rhs, share_start, share_width, 2).astype(jnp.float32)

    def apply_share(left_block, vector_rows):
        on_chip = lax.all_gather(vector_rows, "core", axis=0, tiled=True)
        full_vector = collect(on_chip, "y", 0)
        return local_product(left_block, full_vector)

    first_reduced = (rhs_share[0] - shares[0]).astype(jnp.bfloat16)
    first_solved = apply_share(whole_blocks[0], first_reduced).astype(jnp.bfloat16)
    cross_term = apply_share(whole_blocks[2], first_solved)
    second_reduced = (rhs_share[1] - shares[1] - cross_term).astype(jnp.bfloat16)
    second_solved = apply_share(whole_blocks[1], second_reduced).astype(jnp.bfloat16)
    solved_share = jnp.stack([first_solved, second_solved])
    return collect(solved_share, "col", 2)


def solution(mesh):
    nrow, ncol = mesh.devices.shape
    fine = Mesh(mesh.devices.reshape(nrow // 2, 2, ncol), ("y", "core", "col"))
    return jax.shard_map(
        on_device,
        mesh=fine,
        in_specs=(
            P("col", None),
            P("col", None, ROW),
            P(None, ROW, None),
            P("col", ROW),
            P(None, "col", ROW),
        ),
        out_specs=P(None, ROW, None),
        check_vma=False,
    )
```

```python
import jax
import jax.numpy as jnp
from jax import lax
from jax.sharding import PartitionSpec as P


def in_blocks(array, dim, length):
    dims = array.shape
    blocks = array.reshape(*dims[:dim], length, dims[dim] // length, *dims[dim + 1 :])
    return jnp.moveaxis(blocks, dim, 0)


def sum_at_owner(array, axis, dim):
    length = lax.axis_size(axis)
    blocks = lax.all_to_all(in_blocks(array, dim, length), axis, 0, 0, tiled=True)
    return jnp.sum(blocks, axis=0)


def in_order(blocks, dim):
    blocks = jnp.moveaxis(blocks, 0, dim)
    dims = blocks.shape
    return blocks.reshape(*dims[:dim], dims[dim] * dims[dim + 1], *dims[dim + 2 :])


def sent_to_all(array, axis):
    copies = jnp.broadcast_to(array, (lax.axis_size(axis), *array.shape))
    return lax.all_to_all(copies, axis, split_axis=0, concat_axis=0, tiled=True)


def collect(array, axis, dim):
    return in_order(sent_to_all(array, axis), dim)


def local_product(left_block, right_rows):
    return lax.dot_general(
        left_block, right_rows, (((0,), (0,)), ((), ())), preferred_element_type=jnp.float32
    )


def on_device(prior_solved, lower_prior, rhs, coupling, inverse_diag):
    share_width = rhs.shape[2] // lax.axis_size("col")
    share_start = lax.axis_index("col") * share_width
    stacked = jnp.concatenate([inverse_diag, coupling[None]], axis=0)
    whole_blocks = lax.all_gather(stacked, "col", axis=1, tiled=True)
    depth, blocks, rows = lower_prior.shape
    both_terms = local_product(lower_prior.reshape(depth, blocks * rows), prior_solved)
    both_terms = both_terms.reshape(blocks, rows, rhs.shape[2])
    length = lax.axis_size("col")
    blocks_out = lax.all_to_all(in_blocks(both_terms.astype(jnp.bfloat16), 2, length), "col", 0, 0, tiled=True)
    shares = jnp.sum(blocks_out.astype(jnp.float32), axis=0)
    rhs_share = lax.dynamic_slice_in_dim(rhs, share_start, share_width, 2).astype(jnp.float32)

    def apply_share(left_block, vector_rows):
        full_vector = collect(vector_rows, "row", 0)
        return local_product(left_block, full_vector)

    first_reduced = (rhs_share[0] - shares[0]).astype(jnp.bfloat16)
    first_solved = apply_share(whole_blocks[0], first_reduced).astype(jnp.bfloat16)
    cross_term = apply_share(whole_blocks[2], first_solved)
    second_reduced = (rhs_share[1] - shares[1] - cross_term).astype(jnp.bfloat16)
    second_solved = apply_share(whole_blocks[1], second_reduced).astype(jnp.bfloat16)
    solved_share = jnp.stack([first_solved, second_solved])
    return collect(solved_share, "col", 2)


def solution(mesh):
    return jax.shard_map(
        on_device,
        mesh=mesh,
        in_specs=(
            P("col", None),
            P("col", None, "row"),
            P(None, "row", None),
            P("col", "row"),
            P(None, "col", "row"),
        ),
        out_specs=P(None, "row", None),
        check_vma=False,
    )
```

```python
import jax
import jax.numpy as jnp
from jax import lax
from jax.sharding import PartitionSpec as P


def in_blocks(array, dim, length):
    dims = array.shape
    blocks = array.reshape(*dims[:dim], length, dims[dim] // length, *dims[dim + 1 :])
    return jnp.moveaxis(blocks, dim, 0)


def sum_at_owner(array, axis, dim):
    length = lax.axis_size(axis)
    blocks = lax.all_to_all(in_blocks(array, dim, length), axis, 0, 0, tiled=True)
    return jnp.sum(blocks, axis=0)


def in_order(blocks, dim):
    blocks = jnp.moveaxis(blocks, 0, dim)
    dims = blocks.shape
    return blocks.reshape(*dims[:dim], dims[dim] * dims[dim + 1], *dims[dim + 2 :])


def sent_to_all(array, axis):
    copies = jnp.broadcast_to(array, (lax.axis_size(axis), *array.shape))
    return lax.all_to_all(copies, axis, split_axis=0, concat_axis=0, tiled=True)


def collect(array, axis, dim):
    return in_order(sent_to_all(array, axis), dim)


def local_product(left_block, right_rows):
    return lax.dot_general(
        left_block, right_rows, (((0,), (0,)), ((), ())), preferred_element_type=jnp.float32
    )


def on_device(prior_solved, lower_prior, rhs, coupling, inverse_diag):
    share_width = rhs.shape[2] // lax.axis_size("col")
    share_start = lax.axis_index("col") * share_width
    rows = coupling.shape[1]
    side = jnp.concatenate([inverse_diag[0], inverse_diag[1], coupling], axis=1)
    whole = lax.all_gather(side, "col", axis=0, tiled=True)
    whole_blocks = [whole[:, k * rows : (k + 1) * rows] for k in range(3)]
    depth, blocks, _ = lower_prior.shape
    both_terms = local_product(lower_prior.reshape(depth, blocks * rows), prior_solved)
    both_terms = both_terms.reshape(blocks, rows, rhs.shape[2])
    shares = sum_at_owner(both_terms, "col", 2)
    rhs_share = lax.dynamic_slice_in_dim(rhs, share_start, share_width, 2).astype(jnp.float32)

    def apply_share(left_block, vector_rows):
        full_vector = collect(vector_rows, "row", 0)
        return local_product(left_block, full_vector)

    first_reduced = (rhs_share[0] - shares[0]).astype(jnp.bfloat16)
    first_solved = apply_share(whole_blocks[0], first_reduced).astype(jnp.bfloat16)
    cross_term = apply_share(whole_blocks[2], first_solved)
    second_reduced = (rhs_share[1] - shares[1] - cross_term).astype(jnp.bfloat16)
    second_solved = apply_share(whole_blocks[1], second_reduced).astype(jnp.bfloat16)
    solved_share = jnp.stack([first_solved, second_solved])
    return collect(solved_share, "col", 2)


def solution(mesh):
    return jax.shard_map(
        on_device,
        mesh=mesh,
        in_specs=(
            P("col", None),
            P("col", None, "row"),
            P(None, "row", None),
            P("col", "row"),
            P(None, "col", "row"),
        ),
        out_specs=P(None, "row", None),
        check_vma=False,
    )
```

```python
import jax
import jax.numpy as jnp
from jax import lax
from jax.sharding import Mesh, PartitionSpec as P

COL = ("z", "x")


def in_blocks(array, dim, length):
    dims = array.shape
    blocks = array.reshape(*dims[:dim], length, dims[dim] // length, *dims[dim + 1 :])
    return jnp.moveaxis(blocks, dim, 0)


def sum_at_owner(array, axis, dim):
    length = lax.axis_size(axis)
    blocks = lax.all_to_all(in_blocks(array, dim, length), axis, 0, 0, tiled=True)
    return jnp.sum(blocks, axis=0)


def in_order(blocks, dim):
    blocks = jnp.moveaxis(blocks, 0, dim)
    dims = blocks.shape
    return blocks.reshape(*dims[:dim], dims[dim] * dims[dim + 1], *dims[dim + 2 :])


def sent_to_all(array, axis):
    copies = jnp.broadcast_to(array, (lax.axis_size(axis), *array.shape))
    return lax.all_to_all(copies, axis, split_axis=0, concat_axis=0, tiled=True)


def collect(array, axis, dim):
    return in_order(sent_to_all(array, axis), dim)


def local_product(left_block, right_rows):
    return lax.dot_general(
        left_block, right_rows, (((0,), (0,)), ((), ())), preferred_element_type=jnp.float32
    )


def on_device(prior_solved, lower_prior, rhs, coupling, inverse_diag):
    share_width = rhs.shape[2] // lax.axis_size(COL)
    share_start = lax.axis_index(COL) * share_width
    stacked = jnp.concatenate([inverse_diag, coupling[None]], axis=0)
    whole_blocks = lax.all_gather(stacked, COL, axis=1, tiled=True)
    depth, blocks, rows = lower_prior.shape
    both_terms = local_product(lower_prior.reshape(depth, blocks * rows), prior_solved)
    both_terms = both_terms.reshape(blocks, rows, rhs.shape[2])
    nz, nx = lax.axis_size("z"), lax.axis_size("x")
    per_x = both_terms.reshape(blocks, rows, nz, nx, share_width)
    per_x = jnp.moveaxis(per_x, 3, 0)
    along_x = jnp.sum(lax.all_to_all(per_x, "x", 0, 0, tiled=True), axis=0)
    per_z = jnp.moveaxis(along_x.reshape(blocks, rows, nz, share_width), 2, 0)
    shares = jnp.sum(lax.all_to_all(per_z, "z", 0, 0, tiled=True), axis=0)
    rhs_share = lax.dynamic_slice_in_dim(rhs, share_start, share_width, 2).astype(jnp.float32)

    def apply_share(left_block, vector_rows):
        full_vector = collect(vector_rows, "row", 0)
        return local_product(left_block, full_vector)

    first_reduced = (rhs_share[0] - shares[0]).astype(jnp.bfloat16)
    first_solved = apply_share(whole_blocks[0], first_reduced).astype(jnp.bfloat16)
    cross_term = apply_share(whole_blocks[2], first_solved)
    second_reduced = (rhs_share[1] - shares[1] - cross_term).astype(jnp.bfloat16)
    second_solved = apply_share(whole_blocks[1], second_reduced).astype(jnp.bfloat16)
    solved_share = jnp.stack([first_solved, second_solved])
    return collect(solved_share, COL, 2)


def solution(mesh):
    nrow, ncol = mesh.devices.shape
    fine = Mesh(mesh.devices.reshape(nrow, nrow, ncol // nrow), ("row", "z", "x"))
    return jax.shard_map(
        on_device,
        mesh=fine,
        in_specs=(
            P(COL, None),
            P(COL, None, "row"),
            P(None, "row", None),
            P(COL, "row"),
            P(None, COL, "row"),
        ),
        out_specs=P(None, "row", None),
        check_vma=False,
    )
```
